512 devices in a mesh: dp: 8 (over y), seq: 64 (over z, x, core).
Axes of the slice: x: 4, y: 8, z: 8, core: 2. Of those that a mesh axis runs over, the one named last changes fastest.
Arguments:
- queries: bfloat16 [8, 8192, 2048], P('dp', 'seq'), may hold values from -6 to 6
- keys: bfloat16 [8, 8192, 2048], P('dp', 'seq'), may hold values from -6 to 6
- values: bfloat16 [8, 8192, 2048], P('dp', 'seq'), may hold values from -6 to 6
- lengths: int32 [8], P('dp'), may hold values from 2048 to 8192, as said below
- norm_gain: float32 [2048], replicated, may hold values from 0.1 to 1.9
- out_weight: bfloat16 [2048, 2048], P('seq', 'dp'), may hold values from -0.125 to 0.125
Outputs:
- projected: bfloat16 [8, 8192, 2048], P('dp', 'seq')
The draws below stay inside these ranges and needn't reach their ends.
Inputs may be any that keep to these rules, and one draw needn't show every extreme that they name: `lengths`: each length is a multiple of 128; in every draw some document has the full 8192 tokens.
All inputs are finite; a program needn't handle non-finite values.
Results may differ from the reference program's by a relative error of at most 0.005.
Values may be sent and summed in bfloat16 or wider, within the bound.
No kernel may reach another device: no remote copies, remote signals or barrier semaphores. Data moves between devices by JAX's collectives and lax.ppermute only.
A program may use at most 192 MiB of HBM per device.

```python
import jax
import jax.numpy as jnp
from jax import lax

HEADS = 16
HEAD = 128
OUTW = 2048
BLOCK = 128
HIDDEN_WIDTH = 2048
TOKENS = 8192
GROUPS = 8


def draw_lengths(key, part):
    nblocks = TOKENS // BLOCK
    lowest = max(1, nblocks // 4)
    first_key = jax.random.fold_in(key, 11)
    second_key = jax.random.fold_in(key, 23)
    counts = jax.random.randint(first_key, (GROUPS,), lowest, nblocks)
    chosen = jax.random.randint(second_key, (), 0, GROUPS)
    counts = jnp.where(jnp.arange(GROUPS) == chosen, nblocks, counts)
    return (counts * BLOCK).astype(jnp.int32)


def shard_levels(own_key, dims, shards, least, largest):
    def one(axis_at, shards_of):
        heights = jax.random.uniform(jax.random.fold_in(jax.random.fold_in(own_key, 6), axis_at), (shards_of,), jnp.float32, least / len(shards), largest / len(shards))
        return jnp.repeat(jnp.exp(heights), dims[axis_at] // shards_of).reshape((-1,) + (1,) * (len(dims) - axis_at - 1))

    gain = one(*shards[0])
    for cut in shards[1:]:
        gain = gain * one(*cut)
    return gain


def noise(rng, extent, spread, most, cuts=(), dtype=jnp.bfloat16):
    drawn = jax.random.normal(rng, extent, jnp.float32) * spread
    if len(cuts) > 0:
        drawn = shard_levels(rng, extent, cuts, -0.22, 0.18) * drawn
    return jnp.clip(drawn, min=-most, max=most).astype(dtype)


def setup_inputs(seed: int = 0) -> dict:
    streams_of = jax.random.split(jax.random.key(seed), 7)
    return {
        "queries": noise(streams_of[0], (GROUPS, TOKENS, HIDDEN_WIDTH), 1.0, 6.0, ((0, 8), (1, 64))),
        "keys": noise(streams_of[1], (GROUPS, TOKENS, HIDDEN_WIDTH), 1.0, 6.0, ((0, 8), (1, 64))),
        "values": noise(streams_of[2], (GROUPS, TOKENS, HIDDEN_WIDTH), 1.0, 6.0, ((0, 8), (1, 64))),
        "lengths": draw_lengths(jax.random.fold_in(streams_of[6], 71), 0),
        "norm_gain": jnp.clip(1.0 + 0.18 * jax.random.normal(streams_of[4], (HIDDEN_WIDTH,), jnp.float32), 0.1, 1.9),
        "out_weight": noise(streams_of[5], (HIDDEN_WIDTH, OUTW), HIDDEN_WIDTH ** -0.5, 0.125, ((0, 64), (1, 8))),
    }


def run_document(query_doc, key_doc, value_doc, length, norm_gain, out_weight):
    nblk = TOKENS // BLOCK
    shape = (nblk, BLOCK, HEADS, HEAD)
    query_blocks = query_doc.reshape(shape)
    key_blocks = key_doc.reshape(shape)
    value_blocks = value_doc.reshape(shape)
    causal = jnp.arange(BLOCK)[:, None] >= jnp.arange(BLOCK)[None, :]
    high = lax.Precision.HIGHEST

    def step(state, block):
        query_b, key_b, value_b = block
        query_f = query_b.astype(jnp.float32)
        key_f = key_b.astype(jnp.float32)
        value_f = value_b.astype(jnp.float32)
        scores = jnp.einsum('thd,shd->hts', query_f, key_f, precision=high)
        scores = jnp.where(causal[None], scores, 0.0).astype(jnp.bfloat16)
        local = jnp.einsum('hts,shd->thd', scores.astype(jnp.float32), value_f, precision=high)
        cross = jnp.einsum('thd,hde->the', query_f, state, precision=high)
        state = state + jnp.einsum('shd,she->hde', key_f, value_f, precision=high)
        return (state, local + cross)
    start = jnp.zeros((HEADS, HEAD, HEAD), jnp.float32)
    final_state, mixed = lax.scan(step, start, (query_blocks, key_blocks, value_blocks))
    mixed = mixed.reshape(TOKENS, HEADS, HEAD)
    meansq = lax.optimization_barrier(jnp.mean(mixed * mixed, axis=-1, keepdims=True))
    normed = mixed * lax.rsqrt(meansq + 1e-06) * norm_gain.reshape(HEADS, HEAD)
    valid = jnp.arange(TOKENS) < length
    normed = jnp.where(valid[:, None, None], normed, 0.0).astype(jnp.bfloat16)
    normed = normed.reshape(TOKENS, HEADS * HEAD)
    return jnp.dot(normed, out_weight, preferred_element_type=jnp.float32).astype(jnp.bfloat16)

def reference(queries, keys, values, lengths, norm_gain, out_weight):
    results = []
    for group in range(GROUPS):
        results.append(run_document(queries[group], keys[group], values[group], lengths[group], norm_gain, out_weight))
    return jnp.stack(results)
```

```python
import jax
import jax.numpy as jnp
import numpy as np
from jax import lax
from jax.sharding import Mesh
from jax.sharding import PartitionSpec as P

HEADS = 16
HEAD = 128
BLOCK = 128

SEQ_AXES = ("z", "x", "c")


def exclusive_sum(stack, index):
    mask = jnp.arange(stack.shape[0]) < index
    mask = mask.reshape((-1,) + (1,) * (stack.ndim - 1))
    return jnp.sum(jnp.where(mask, stack, 0.0), axis=0)


def prefix_of(own):
    zi, xi, ci = (lax.axis_index(a) for a in SEQ_AXES)
    nx, nc = lax.axis_size("x"), lax.axis_size("c")
    on_chip = lax.all_gather(own, "c")
    chip_total = jnp.sum(on_chip, axis=0)
    within_chip = exclusive_sum(on_chip, ci)
    half = HEADS // nc
    mine = lax.dynamic_slice_in_dim(chip_total, ci * half, half, 0)
    row = lax.all_gather(mine, "x")
    before_in_row = exclusive_sum(row, xi)
    row_total = jnp.sum(row, axis=0)
    quarter = half // nx
    piece = lax.dynamic_slice_in_dim(row_total, xi * quarter, quarter, 0)
    rows = lax.all_gather(piece, "z")
    before_rows = exclusive_sum(rows, zi)
    before_rows = lax.all_gather(before_rows, "x", axis=0, tiled=True)
    chip_prefix = lax.all_gather(before_rows + before_in_row, "c", axis=0, tiled=True)
    return chip_prefix + within_chip


def body(queries, keys, values, lengths, norm_gain, out_weight):
    nz, nx, nc = (lax.axis_size(a) for a in SEQ_AXES)
    query_doc = queries[0]
    tok = query_doc.shape[0]
    nblk = tok // BLOCK
    shape = (nblk, BLOCK, HEADS, HEAD)
    query_blocks = query_doc.reshape(shape)
    key_blocks = keys[0].reshape(shape)
    value_blocks = values[0].reshape(shape)
    high = lax.Precision.HIGHEST
    block_state = jnp.einsum(
        "nshd,nshe->nhde", key_blocks, value_blocks, preferred_element_type=jnp.float32
    )
    own_state = jnp.sum(block_state, axis=0)
    prefix = prefix_of(own_state)
    running = jnp.cumsum(block_state, axis=0)
    earlier = jnp.concatenate(
        [jnp.zeros((1, HEADS, HEAD, HEAD), jnp.float32), running[:-1]], axis=0
    )
    prior_state = prefix[None] + earlier
    causal = jnp.arange(BLOCK)[:, None] >= jnp.arange(BLOCK)[None, :]
    scores = jnp.einsum(
        "nthd,nshd->nhts", query_blocks, key_blocks, preferred_element_type=jnp.float32
    )
    scores = jnp.where(causal[None, None], scores, 0.0).astype(jnp.bfloat16)
    local = jnp.einsum("nhts,nshd->nthd", scores, value_blocks, preferred_element_type=jnp.float32)
    cross = jnp.einsum(
        "nthd,nhde->nthe", query_blocks.astype(jnp.float32), prior_state, precision=high
    )
    mixed = (local + cross).reshape(tok, HEADS, HEAD)
    meansq = jnp.mean(mixed * mixed, axis=-1, keepdims=True)
    normed = mixed * lax.rsqrt(meansq + 1e-06) * norm_gain.reshape(HEADS, HEAD)
    seq_index = lax.axis_index(SEQ_AXES)
    position = seq_index * tok + jnp.arange(tok)
    valid = position < lengths[0]
    normed = jnp.where(valid[:, None, None], normed, 0.0).astype(jnp.bfloat16)
    rows_per, cols_per = out_weight.shape
    ndp = lax.axis_size("dp")
    gathered = lax.all_gather(out_weight, ("dp", "z", "x"), axis=0)
    gathered = gathered.reshape(ndp, nz, nx, rows_per, cols_per)
    weight = lax.all_gather(gathered, "c", axis=0)
    normed = normed.reshape(tok, nz, nx, nc, rows_per)
    result = jnp.einsum(
        "tzxcr,cdzxrk->tdk", normed, weight, preferred_element_type=jnp.float32
    )
    return result.astype(jnp.bfloat16).reshape(tok, ndp * cols_per)[None]


def solution(mesh, nx=4, ncore=2):
    ndp, nseq = mesh.devices.shape
    devices = np.asarray(mesh.devices).reshape(ndp, nseq // (nx * ncore), nx, ncore)
    fine = Mesh(devices, ("dp",) + SEQ_AXES)
    rows = P("dp", SEQ_AXES, None)
    in_specs = (rows, rows, rows, P("dp"), P(), P(SEQ_AXES, "dp"))
    return jax.shard_map(body, mesh=fine, in_specs=in_specs, out_specs=rows, check_vma=False)
```

```python
import jax
import jax.numpy as jnp
import numpy as np
from jax import lax
from jax.sharding import Mesh
from jax.sharding import PartitionSpec as P

HEADS = 16
HEAD = 128
BLOCK = 128

SEQ_AXES = ("z", "x", "c")


def exclusive_cumsum(stack):
    running = jnp.cumsum(stack, axis=0)
    return jnp.concatenate([jnp.zeros_like(stack[:1]), running[:-1]], axis=0), running[-1]


def swap_cores(x):
    return lax.ppermute(x, "c", [(0, 1), (1, 0)])


def prefix_of(own):
    xi, ci = lax.axis_index("x"), lax.axis_index("c")
    nz, nx, nc = (lax.axis_size(a) for a in SEQ_AXES)
    assert nc == 2
    partner = swap_cores(own)
    chip_total = own + partner
    within_chip = jnp.where(ci == 1, partner, jnp.zeros_like(partner))
    half = HEADS // nc
    quarter = half // nx
    mine = lax.dynamic_slice_in_dim(chip_total, ci * half, half, 0)
    by_chip = lax.all_to_all(mine.reshape(nx, quarter, HEAD, HEAD), "x", 0, 0)
    before_in_row, row_total = exclusive_cumsum(by_chip)
    pieces = row_total.reshape(nz, quarter * HEAD // nz, HEAD)
    by_row = lax.all_to_all(pieces, "z", 0, 0)
    before_rows, _ = exclusive_cumsum(by_row)
    before_rows = lax.all_to_all(before_rows, "z", 0, 0).reshape(quarter, HEAD, HEAD)
    back = lax.all_to_all(before_in_row + before_rows[None], "x", 0, 0)
    mine = back.reshape(half, HEAD, HEAD)
    theirs = swap_cores(mine)
    chip_prefix = jnp.where(
        ci == 0,
        jnp.concatenate([mine, theirs], axis=0),
        jnp.concatenate([theirs, mine], axis=0),
    )
    return chip_prefix + within_chip


def body(queries, keys, values, lengths, norm_gain, out_weight):
    nz, nx, nc = (lax.axis_size(a) for a in SEQ_AXES)
    query_doc = queries[0]
    tok = query_doc.shape[0]
    nblk = tok // BLOCK
    shape = (nblk, BLOCK, HEADS, HEAD)
    query_blocks = query_doc.reshape(shape)
    key_blocks = keys[0].reshape(shape)
    value_blocks = values[0].reshape(shape)
    high = lax.Precision.HIGHEST
    block_state = jnp.einsum(
        "nshd,nshe->nhde", key_blocks, value_blocks, preferred_element_type=jnp.float32
    )
    own_state = jnp.sum(block_state, axis=0)
    prefix = prefix_of(own_state)
    running = jnp.cumsum(block_state, axis=0)
    earlier = jnp.concatenate(
        [jnp.zeros((1, HEADS, HEAD, HEAD), jnp.float32), running[:-1]], axis=0
    )
    prior_state = prefix[None] + earlier
    causal = jnp.arange(BLOCK)[:, None] >= jnp.arange(BLOCK)[None, :]
    scores = jnp.einsum(
        "nthd,nshd->nhts", query_blocks, key_blocks, preferred_element_type=jnp.float32
    )
    scores = jnp.where(causal[None, None], scores, 0.0).astype(jnp.bfloat16)
    local = jnp.einsum("nhts,nshd->nthd", scores, value_blocks, preferred_element_type=jnp.float32)
    cross = jnp.einsum(
        "nthd,nhde->nthe", query_blocks.astype(jnp.float32), prior_state, precision=high
    )
    mixed = (local + cross).reshape(tok, HEADS, HEAD)
    meansq = jnp.mean(mixed * mixed, axis=-1, keepdims=True)
    normed = mixed * lax.rsqrt(meansq + 1e-06) * norm_gain.reshape(HEADS, HEAD)
    seq_index = lax.axis_index(SEQ_AXES)
    position = seq_index * tok + jnp.arange(tok)
    valid = position < lengths[0]
    normed = jnp.where(valid[:, None, None], normed, 0.0).astype(jnp.bfloat16)
    rows_per, cols_per = out_weight.shape
    ndp = lax.axis_size("dp")
    ci = lax.axis_index("c")
    wide = lax.all_gather(out_weight, "dp", axis=1, tiled=True)
    own_rows = lax.all_gather(wide, ("z", "x"), axis=0, tiled=True)
    other_rows = swap_cores(own_rows)
    normed = normed.reshape(tok, nz, nx, nc, rows_per)
    normed_own = jnp.take(normed, ci, axis=3).reshape(tok, nz * nx * rows_per)
    normed_other = jnp.take(normed, 1 - ci, axis=3).reshape(tok, nz * nx * rows_per)
    result = jnp.dot(normed_own, own_rows, preferred_element_type=jnp.float32)
    result = result + jnp.dot(normed_other, other_rows, preferred_element_type=jnp.float32)
    return result.astype(jnp.bfloat16)[None]


def solution(mesh, nx=4, ncore=2):
    ndp, nseq = mesh.devices.shape
    devices = np.asarray(mesh.devices).reshape(ndp, nseq // (nx * ncore), nx, ncore)
    fine = Mesh(devices, ("dp",) + SEQ_AXES)
    rows = P("dp", SEQ_AXES, None)
    in_specs = (rows, rows, rows, P("dp"), P(), P(SEQ_AXES, "dp"))
    return jax.shard_map(body, mesh=fine, in_specs=in_specs, out_specs=rows, check_vma=False)
```

```python
import jax
import jax.numpy as jnp
import numpy as np
from jax import lax
from jax.sharding import Mesh
from jax.sharding import PartitionSpec as P

HEADS = 16
HEAD = 128
BLOCK = 128

SEQ_AXES = ("z", "x", "c")


def exclusive_cumsum(stack):
    running = jnp.cumsum(stack, axis=0)
    return jnp.concatenate([jnp.zeros_like(stack[:1]), running[:-1]], axis=0), running[-1]


def swap_cores(x):
    return lax.ppermute(x, "c", [(0, 1), (1, 0)])


def exchange(x, axis):
    n, i = lax.axis_size(axis), lax.axis_index(axis)
    by_offset = [jnp.take(x, i, axis=0)]
    for s in range(1, n):
        sent = jnp.take(x, (i + s) % n, axis=0)
        by_offset.append(lax.ppermute(sent, axis, [(j, (j + s) % n) for j in range(n)]))
    return jnp.take(jnp.stack(by_offset), (i - jnp.arange(n)) % n, axis=0)


def ring_gather(x, axis):
    n, i = lax.axis_size(axis), lax.axis_index(axis)
    forward = [(j, (j + 1) % n) for j in range(n)]
    backward = [(j, (j - 1) % n) for j in range(n)]
    n_left, n_right = n // 2, (n - 1) // 2
    from_left, from_right = [], []
    left = right = x
    for step in range(max(n_left, n_right)):
        if step < n_left:
            left = lax.ppermute(left, axis, forward)
            from_left.append(left)
        if step < n_right:
            right = lax.ppermute(right, axis, backward)
            from_right.append(right)
    by_offset = [x] + from_right + from_left[::-1]
    return jnp.take(jnp.stack(by_offset), (jnp.arange(n) - i) % n, axis=0)


def prefix_of(own):
    xi, ci = lax.axis_index("x"), lax.axis_index("c")
    nz, nx, nc = (lax.axis_size(a) for a in SEQ_AXES)
    assert nc == 2
    partner = swap_cores(own)
    chip_total = own + partner
    within_chip = jnp.where(ci == 1, partner, jnp.zeros_like(partner))
    half = HEADS // nc
    quarter = half // nx
    mine = lax.dynamic_slice_in_dim(chip_total, ci * half, half, 0)
    by_chip = exchange(mine.reshape(nx, quarter, HEAD, HEAD), "x")
    before_in_row, row_total = exclusive_cumsum(by_chip)
    pieces = row_total.reshape(nz, quarter * HEAD // nz, HEAD)
    by_row = exchange(pieces, "z")
    before_rows, _ = exclusive_cumsum(by_row)
    before_rows = exchange(before_rows, "z").reshape(quarter, HEAD, HEAD)
    back = exchange(before_in_row + before_rows[None], "x")
    mine = back.reshape(half, HEAD, HEAD)
    theirs = swap_cores(mine)
    chip_prefix = jnp.where(
        ci == 0,
        jnp.concatenate([mine, theirs], axis=0),
        jnp.concatenate([theirs, mine], axis=0),
    )
    return chip_prefix + within_chip


def body(queries, keys, values, lengths, norm_gain, out_weight):
    nz, nx, nc = (lax.axis_size(a) for a in SEQ_AXES)
    query_doc = queries[0]
    tok = query_doc.shape[0]
    nblk = tok // BLOCK
    shape = (nblk, BLOCK, HEADS, HEAD)
    query_blocks = query_doc.reshape(shape)
    key_blocks = keys[0].reshape(shape)
    value_blocks = values[0].reshape(shape)
    high = lax.Precision.HIGHEST
    block_state = jnp.einsum(
        "nshd,nshe->nhde", key_blocks, value_blocks, preferred_element_type=jnp.float32
    )
    own_state = jnp.sum(block_state, axis=0)
    prefix = prefix_of(own_state)
    running = jnp.cumsum(block_state, axis=0)
    earlier = jnp.concatenate(
        [jnp.zeros((1, HEADS, HEAD, HEAD), jnp.float32), running[:-1]], axis=0
    )
    prior_state = prefix[None] + earlier
    causal = jnp.arange(BLOCK)[:, None] >= jnp.arange(BLOCK)[None, :]
    scores = jnp.einsum(
        "nthd,nshd->nhts", query_blocks, key_blocks, preferred_element_type=jnp.float32
    )
    scores = jnp.where(causal[None, None], scores, 0.0).astype(jnp.bfloat16)
    local = jnp.einsum("nhts,nshd->nthd", scores, value_blocks, preferred_element_type=jnp.float32)
    cross = jnp.einsum(
        "nthd,nhde->nthe", query_blocks.astype(jnp.float32), prior_state, precision=high
    )
    mixed = (local + cross).reshape(tok, HEADS, HEAD)
    meansq = jnp.mean(mixed * mixed, axis=-1, keepdims=True)
    normed = mixed * lax.rsqrt(meansq + 1e-06) * norm_gain.reshape(HEADS, HEAD)
    seq_index = lax.axis_index(SEQ_AXES)
    position = seq_index * tok + jnp.arange(tok)
    valid = position < lengths[0]
    normed = jnp.where(valid[:, None, None], normed, 0.0).astype(jnp.bfloat16)
    rows_per, cols_per = out_weight.shape
    ndp = lax.axis_size("dp")
    ci = lax.axis_index("c")
    split = cols_per // 2
    first = ring_gather(ring_gather(ring_gather(out_weight[:, :split], "dp"), "x"), "z")
    second = ring_gather(ring_gather(ring_gather(out_weight[:, split:], "z"), "x"), "dp")
    first_other = swap_cores(first)
    second_other = swap_cores(second)
    normed = normed.reshape(tok, nz, nx, nc, rows_per)
    normed_own = jnp.take(normed, ci, axis=3)
    normed_other = jnp.take(normed, 1 - ci, axis=3)
    f32 = jnp.float32
    out_first = jnp.einsum("tzxr,zxdrk->tdk", normed_own, first, preferred_element_type=f32)
    out_first = out_first + jnp.einsum(
        "tzxr,zxdrk->tdk", normed_other, first_other, preferred_element_type=f32
    )
    out_second = jnp.einsum("tzxr,dxzrk->tdk", normed_own, second, preferred_element_type=f32)
    out_second = out_second + jnp.einsum(
        "tzxr,dxzrk->tdk", normed_other, second_other, preferred_element_type=f32
    )
    result = jnp.concatenate([out_first, out_second], axis=2)
    return result.astype(jnp.bfloat16).reshape(tok, ndp * cols_per)[None]


def solution(mesh, nx=4, ncore=2):
    ndp, nseq = mesh.devices.shape
    devices = np.asarray(mesh.devices).reshape(ndp, nseq // (nx * ncore), nx, ncore)
    fine = Mesh(devices, ("dp",) + SEQ_AXES)
    rows = P("dp", SEQ_AXES, None)
    in_specs = (rows, rows, rows, P("dp"), P(), P(SEQ_AXES, "dp"))
    return jax.shard_map(body, mesh=fine, in_specs=in_specs, out_specs=rows, check_vma=False)
```

```python
import jax
import jax.numpy as jnp
import numpy as np
from jax import lax
from jax.sharding import Mesh
from jax.sharding import PartitionSpec as P

HEADS = 16
HEAD = 128
BLOCK = 128

SEQ_AXES = ("z", "x", "c")


def exclusive_cumsum(stack):
    running = jnp.cumsum(stack, axis=0)
    return jnp.concatenate([jnp.zeros_like(stack[:1]), running[:-1]], axis=0), running[-1]


def swap_cores(x):
    return lax.ppermute(x, "c", [(0, 1), (1, 0)])


def prefix_of(own):
    ci = lax.axis_index("c")
    nz, nx, nc = (lax.axis_size(a) for a in SEQ_AXES)
    assert nc == 2
    partner = swap_cores(own)
    chip_total = own + partner
    within_chip = jnp.where(ci == 1, partner, jnp.zeros_like(partner))
    half = HEADS // nc
    chips = nz * nx
    mine = lax.dynamic_slice_in_dim(chip_total, ci * half, half, 0)
    pieces = mine.reshape(chips, half * HEAD // chips, HEAD)
    by_chip = lax.all_to_all(pieces, ("z", "x"), 0, 0)
    before, _ = exclusive_cumsum(by_chip)
    back = lax.all_to_all(before, ("z", "x"), 0, 0)
    mine = back.reshape(half, HEAD, HEAD)
    theirs = swap_cores(mine)
    chip_prefix = jnp.where(
        ci == 0,
        jnp.concatenate([mine, theirs], axis=0),
        jnp.concatenate([theirs, mine], axis=0),
    )
    return chip_prefix + within_chip


def body(queries, keys, values, lengths, norm_gain, out_weight):
    nz, nx, nc = (lax.axis_size(a) for a in SEQ_AXES)
    query_doc = queries[0]
    tok = query_doc.shape[0]
    nblk = tok // BLOCK
    shape = (nblk, BLOCK, HEADS, HEAD)
    query_blocks = query_doc.reshape(shape)
    key_blocks = keys[0].reshape(shape)
    value_blocks = values[0].reshape(shape)
    high = lax.Precision.HIGHEST
    block_state = jnp.einsum(
        "nshd,nshe->nhde", key_blocks, value_blocks, preferred_element_type=jnp.float32
    )
    own_state = jnp.sum(block_state, axis=0)
    prefix = prefix_of(own_state)
    running = jnp.cumsum(block_state, axis=0)
    earlier = jnp.concatenate(
        [jnp.zeros((1, HEADS, HEAD, HEAD), jnp.float32), running[:-1]], axis=0
    )
    prior_state = prefix[None] + earlier
    causal = jnp.arange(BLOCK)[:, None] >= jnp.arange(BLOCK)[None, :]
    scores = jnp.einsum(
        "nthd,nshd->nhts", query_blocks, key_blocks, preferred_element_type=jnp.float32
    )
    scores = jnp.where(causal[None, None], scores, 0.0).astype(jnp.bfloat16)
    local = jnp.einsum("nhts,nshd->nthd", scores, value_blocks, preferred_element_type=jnp.float32)
    cross = jnp.einsum(
        "nthd,nhde->nthe", query_blocks.astype(jnp.float32), prior_state, precision=high
    )
    mixed = (local + cross).reshape(tok, HEADS, HEAD)
    meansq = jnp.mean(mixed * mixed, axis=-1, keepdims=True)
    normed = mixed * lax.rsqrt(meansq + 1e-06) * norm_gain.reshape(HEADS, HEAD)
    seq_index = lax.axis_index(SEQ_AXES)
    position = seq_index * tok + jnp.arange(tok)
    valid = position < lengths[0]
    normed = jnp.where(valid[:, None, None], normed, 0.0).astype(jnp.bfloat16)
    rows_per, cols_per = out_weight.shape
    ndp = lax.axis_size("dp")
    copies = jnp.broadcast_to(out_weight[None], (ndp, rows_per, cols_per))
    by_column = lax.all_to_all(copies, "dp", 0, 0)
    wide = jnp.transpose(by_column, (1, 0, 2)).reshape(rows_per, ndp * cols_per)
    weight = lax.all_gather(wide, SEQ_AXES, axis=0, tiled=True)
    normed = normed.reshape(tok, HEADS * HEAD)
    result = jnp.dot(normed, weight, preferred_element_type=jnp.float32)
    return result.astype(jnp.bfloat16)[None]


def solution(mesh, nx=4, ncore=2):
    ndp, nseq = mesh.devices.shape
    devices = np.asarray(mesh.devices).reshape(ndp, nseq // (nx * ncore), nx, ncore)
    fine = Mesh(devices, ("dp",) + SEQ_AXES)
    rows = P("dp", SEQ_AXES, None)
    in_specs = (rows, rows, rows, P("dp"), P(), P(SEQ_AXES, "dp"))
    return jax.shard_map(body, mesh=fine, in_specs=in_specs, out_specs=rows, check_vma=False)
```

```python
import jax
import jax.numpy as jnp
import numpy as np
from jax import lax
from jax.sharding import Mesh
from jax.sharding import PartitionSpec as P

HEADS = 16
HEAD = 128
BLOCK = 128

SEQ_AXES = ("z", "x", "c")


def exclusive_cumsum(stack):
    running = jnp.cumsum(stack, axis=0)
    return jnp.concatenate([jnp.zeros_like(stack[:1]), running[:-1]], axis=0), running[-1]


def swap_cores(x):
    return lax.ppermute(x, "c", [(0, 1), (1, 0)])


def doubling_gather(x, axis):
    n, i = lax.axis_size(axis), lax.axis_index(axis)
    block = x[None]
    step = 1
    while step < n:
        partner = lax.ppermute(block, axis, [(j, j ^ step) for j in range(n)])
        low = (i & step) == 0
        block = jnp.where(
            low,
            jnp.concatenate([block, partner], axis=0),
            jnp.concatenate([partner, block], axis=0),
        )
        step *= 2
    return block


def prefix_of(own):
    ci = lax.axis_index("c")
    nz, nx, nc = (lax.axis_size(a) for a in SEQ_AXES)
    assert nc == 2
    partner = swap_cores(own)
    chip_total = own + partner
    within_chip = jnp.where(ci == 1, partner, jnp.zeros_like(partner))
    half = HEADS // nc
    chips = nz * nx
    mine = lax.dynamic_slice_in_dim(chip_total, ci * half, half, 0)
    pieces = mine.reshape(chips, half * HEAD // chips, HEAD)
    by_chip = lax.all_to_all(pieces, ("z", "x"), 0, 0)
    before, _ = exclusive_cumsum(by_chip)
    back = lax.all_to_all(before, ("z", "x"), 0, 0)
    mine = back.reshape(half, HEAD, HEAD)
    theirs = swap_cores(mine)
    chip_prefix = jnp.where(
        ci == 0,
        jnp.concatenate([mine, theirs], axis=0),
        jnp.concatenate([theirs, mine], axis=0),
    )
    return chip_prefix + within_chip


def body(queries, keys, values, lengths, norm_gain, out_weight):
    nz, nx, nc = (lax.axis_size(a) for a in SEQ_AXES)
    query_doc = queries[0]
    tok = query_doc.shape[0]
    nblk = tok // BLOCK
    shape = (nblk, BLOCK, HEADS, HEAD)
    query_blocks = query_doc.reshape(shape)
    key_blocks = keys[0].reshape(shape)
    value_blocks = values[0].reshape(shape)
    high = lax.Precision.HIGHEST
    block_state = jnp.einsum(
        "nshd,nshe->nhde", key_blocks, value_blocks, preferred_element_type=jnp.float32
    )
    own_state = jnp.sum(block_state, axis=0)
    prefix = prefix_of(own_state)
    running = jnp.cumsum(block_state, axis=0)
    earlier = jnp.concatenate(
        [jnp.zeros((1, HEADS, HEAD, HEAD), jnp.float32), running[:-1]], axis=0
    )
    prior_state = prefix[None] + earlier
    causal = jnp.arange(BLOCK)[:, None] >= jnp.arange(BLOCK)[None, :]
    scores = jnp.einsum(
        "nthd,nshd->nhts", query_blocks, key_blocks, preferred_element_type=jnp.float32
    )
    scores = jnp.where(causal[None, None], scores, 0.0).astype(jnp.bfloat16)
    local = jnp.einsum("nhts,nshd->nthd", scores, value_blocks, preferred_element_type=jnp.float32)
    cross = jnp.einsum(
        "nthd,nhde->nthe", query_blocks.astype(jnp.float32), prior_state, precision=high
    )
    mixed = (local + cross).reshape(tok, HEADS, HEAD)
    meansq = jnp.mean(mixed * mixed, axis=-1, keepdims=True)
    normed = mixed * lax.rsqrt(meansq + 1e-06) * norm_gain.reshape(HEADS, HEAD)
    seq_index = lax.axis_index(SEQ_AXES)
    position = seq_index * tok + jnp.arange(tok)
    valid = position < lengths[0]
    normed = jnp.where(valid[:, None, None], normed, 0.0).astype(jnp.bfloat16)
    rows_per, cols_per = out_weight.shape
    ndp = lax.axis_size("dp")
    by_column = doubling_gather(out_weight, "dp")
    wide = jnp.transpose(by_column, (1, 0, 2)).reshape(rows_per, ndp * cols_per)
    weight = lax.all_gather(wide, SEQ_AXES, axis=0, tiled=True)
    normed = normed.reshape(tok, HEADS * HEAD)
    result = jnp.dot(normed, weight, preferred_element_type=jnp.float32)
    return result.astype(jnp.bfloat16)[None]


def solution(mesh, nx=4, ncore=2):
    ndp, nseq = mesh.devices.shape
    devices = np.asarray(mesh.devices).reshape(ndp, nseq // (nx * ncore), nx, ncore)
    fine = Mesh(devices, ("dp",) + SEQ_AXES)
    rows = P("dp", SEQ_AXES, None)
    in_specs = (rows, rows, rows, P("dp"), P(), P(SEQ_AXES, "dp"))
    return jax.shard_map(body, mesh=fine, in_specs=in_specs, out_specs=rows, check_vma=False)
```

```python
import jax
import jax.numpy as jnp
import numpy as np
from jax import lax
from jax.sharding import Mesh
from jax.sharding import PartitionSpec as P

HEADS = 16
HEAD = 128
BLOCK = 128

SEQ_AXES = ("z", "x", "c")


def exclusive_cumsum(stack):
    running = jnp.cumsum(stack, axis=0)
    return jnp.concatenate([jnp.zeros_like(stack[:1]), running[:-1]], axis=0), running[-1]


def swap_cores(x):
    return lax.ppermute(x, "c", [(0, 1), (1, 0)])


def prefix_of(own):
    ci = lax.axis_index("c")
    nz, nx, nc = (lax.axis_size(a) for a in SEQ_AXES)
    assert nc == 2
    partner = swap_cores(own)
    chip_total = own + partner
    within_chip = jnp.where(ci == 1, partner, jnp.zeros_like(partner))
    half = HEADS // nc
    chips = nz * nx
    mine = lax.dynamic_slice_in_dim(chip_total, ci * half, half, 0)
    pieces = mine.reshape(chips, half * HEAD // chips, HEAD)
    by_chip = lax.all_to_all(pieces, ("z", "x"), 0, 0)
    before, _ = exclusive_cumsum(by_chip)
    back = lax.all_to_all(before, ("z", "x"), 0, 0)
    mine = back.reshape(half, HEAD, HEAD)
    theirs = swap_cores(mine)
    chip_prefix = jnp.where(
        ci == 0,
        jnp.concatenate([mine, theirs], axis=0),
        jnp.concatenate([theirs, mine], axis=0),
    )
    return chip_prefix + within_chip


def body(queries, keys, values, lengths, norm_gain, out_weight):
    nz, nx, nc = (lax.axis_size(a) for a in SEQ_AXES)
    query_doc = queries[0]
    tok = query_doc.shape[0]
    nblk = tok // BLOCK
    shape = (nblk, BLOCK, HEADS, HEAD)
    query_blocks = query_doc.reshape(shape)
    key_blocks = keys[0].reshape(shape)
    value_blocks = values[0].reshape(shape)
    high = lax.Precision.HIGHEST
    block_state = jnp.einsum(
        "nshd,nshe->nhde", key_blocks, value_blocks, preferred_element_type=jnp.float32
    )
    own_state = jnp.sum(block_state, axis=0)
    prefix = prefix_of(own_state)
    running = jnp.cumsum(block_state, axis=0)
    earlier = jnp.concatenate(
        [jnp.zeros((1, HEADS, HEAD, HEAD), jnp.float32), running[:-1]], axis=0
    )
    prior_state = prefix[None] + earlier
    causal = jnp.arange(BLOCK)[:, None] >= jnp.arange(BLOCK)[None, :]
    scores = jnp.einsum(
        "nthd,nshd->nhts", query_blocks, key_blocks, preferred_element_type=jnp.float32
    )
    scores = jnp.where(causal[None, None], scores, 0.0).astype(jnp.bfloat16)
    local = jnp.einsum("nhts,nshd->nthd", scores, value_blocks, preferred_element_type=jnp.float32)
    cross = jnp.einsum(
        "nthd,nhde->nthe", query_blocks.astype(jnp.float32), prior_state, precision=high
    )
    mixed = (local + cross).reshape(tok, HEADS, HEAD)
    meansq = jnp.mean(mixed * mixed, axis=-1, keepdims=True)
    normed = mixed * lax.rsqrt(meansq + 1e-06) * norm_gain.reshape(HEADS, HEAD)
    seq_index = lax.axis_index(SEQ_AXES)
    position = seq_index * tok + jnp.arange(tok)
    valid = position < lengths[0]
    normed = jnp.where(valid[:, None, None], normed, 0.0).astype(jnp.bfloat16)
    rows_per, cols_per = out_weight.shape
    ndp = lax.axis_size("dp")
    by_row = lax.all_to_all(
        jnp.broadcast_to(out_weight[None], (nz, rows_per, cols_per)), "z", 0, 0
    )
    by_column = lax.all_to_all(
        jnp.broadcast_to(by_row[None], (ndp, nz, rows_per, cols_per)), "dp", 0, 0
    )
    block = jnp.transpose(by_column, (1, 2, 0, 3)).reshape(nz * rows_per, ndp * cols_per)
    weight = lax.all_gather(block, ("x", "c"), axis=0, tiled=True)
    normed = normed.reshape(tok, nz, nx, nc, rows_per).transpose(0, 2, 3, 1, 4)
    normed = normed.reshape(tok, HEADS * HEAD)
    result = jnp.dot(normed, weight, preferred_element_type=jnp.float32)
    return result.astype(jnp.bfloat16)[None]


def solution(mesh, nx=4, ncore=2):
    ndp, nseq = mesh.devices.shape
    devices = np.asarray(mesh.devices).reshape(ndp, nseq // (nx * ncore), nx, ncore)
    fine = Mesh(devices, ("dp",) + SEQ_AXES)
    rows = P("dp", SEQ_AXES, None)
    in_specs = (rows, rows, rows, P("dp"), P(), P(SEQ_AXES, "dp"))
    return jax.shard_map(body, mesh=fine, in_specs=in_specs, out_specs=rows, check_vma=False)
```

```python
import jax
import jax.numpy as jnp
import numpy as np
from jax import lax
from jax.sharding import Mesh
from jax.sharding import PartitionSpec as P

HEADS = 16
HEAD = 128
BLOCK = 128

SEQ_AXES = ("z", "x", "c")


def exclusive_cumsum(stack):
    running = jnp.cumsum(stack, axis=0)
    return jnp.concatenate([jnp.zeros_like(stack[:1]), running[:-1]], axis=0), running[-1]


def swap_cores(x):
    return lax.ppermute(x, "c", [(0, 1), (1, 0)])


def prefix_of(own):
    ci = lax.axis_index("c")
    nz, nx, nc = (lax.axis_size(a) for a in SEQ_AXES)
    assert nc == 2
    partner = swap_cores(own)
    chip_total = own + partner
    within_chip = jnp.where(ci == 1, partner, jnp.zeros_like(partner))
    half = HEADS // nc
    chips = nz * nx
    mine = lax.dynamic_slice_in_dim(chip_total, ci * half, half, 0)
    pieces = mine.reshape(chips, half * HEAD // chips, HEAD)
    by_chip = lax.all_to_all(pieces, ("z", "x"), 0, 0)
    before, _ = exclusive_cumsum(by_chip)
    back = lax.all_to_all(before, ("z", "x"), 0, 0)
    mine = back.reshape(half, HEAD, HEAD)
    theirs = swap_cores(mine)
    chip_prefix = jnp.where(
        ci == 0,
        jnp.concatenate([mine, theirs], axis=0),
        jnp.concatenate([theirs, mine], axis=0),
    )
    return chip_prefix + within_chip


def body(queries, keys, values, lengths, norm_gain, out_weight):
    nz, nx, nc = (lax.axis_size(a) for a in SEQ_AXES)
    query_doc = queries[0]
    tok = query_doc.shape[0]
    nblk = tok // BLOCK
    shape = (nblk, BLOCK, HEADS, HEAD)
    query_blocks = query_doc.reshape(shape)
    key_blocks = keys[0].reshape(shape)
    value_blocks = values[0].reshape(shape)
    high = lax.Precision.HIGHEST
    block_state = jnp.einsum(
        "nshd,nshe->nhde", key_blocks, value_blocks, preferred_element_type=jnp.float32
    )
    own_state = jnp.sum(block_state, axis=0)
    prefix = prefix_of(own_state)
    running = jnp.cumsum(block_state, axis=0)
    earlier = jnp.concatenate(
        [jnp.zeros((1, HEADS, HEAD, HEAD), jnp.float32), running[:-1]], axis=0
    )
    prior_state = prefix[None] + earlier
    causal = jnp.arange(BLOCK)[:, None] >= jnp.arange(BLOCK)[None, :]
    scores = jnp.einsum(
        "nthd,nshd->nhts", query_blocks, key_blocks, preferred_element_type=jnp.float32
    )
    scores = jnp.where(causal[None, None], scores, 0.0).astype(jnp.bfloat16)
    local = jnp.einsum("nhts,nshd->nthd", scores, value_blocks, preferred_element_type=jnp.float32)
    cross = jnp.einsum(
        "nthd,nhde->nthe", query_blocks.astype(jnp.float32), prior_state, precision=high
    )
    mixed = (local + cross).reshape(tok, HEADS, HEAD)
    meansq = jnp.mean(mixed * mixed, axis=-1, keepdims=True)
    normed = mixed * lax.rsqrt(meansq + 1e-06) * norm_gain.reshape(HEADS, HEAD)
    seq_index = lax.axis_index(SEQ_AXES)
    position = seq_index * tok + jnp.arange(tok)
    valid = position < lengths[0]
    normed = jnp.where(valid[:, None, None], normed, 0.0).astype(jnp.bfloat16)
    rows_per, cols_per = out_weight.shape
    ndp = lax.axis_size("dp")
    copies = jnp.broadcast_to(out_weight[None], (nz * ndp, rows_per, cols_per))
    by_peer = lax.all_to_all(copies, ("z", "dp"), 0, 0).reshape(nz, ndp, rows_per, cols_per)
    block = jnp.transpose(by_peer, (0, 2, 1, 3)).reshape(nz * rows_per, ndp * cols_per)
    weight = lax.all_gather(block, ("x", "c"), axis=0, tiled=True)
    normed = normed.reshape(tok, nz, nx, nc, rows_per).transpose(0, 2, 3, 1, 4)
    normed = normed.reshape(tok, HEADS * HEAD)
    result = jnp.dot(normed, weight, preferred_element_type=jnp.float32)
    return result.astype(jnp.bfloat16)[None]


def solution(mesh, nx=4, ncore=2):
    ndp, nseq = mesh.devices.shape
    devices = np.asarray(mesh.devices).reshape(ndp, nseq // (nx * ncore), nx, ncore)
    fine = Mesh(devices, ("dp",) + SEQ_AXES)
    rows = P("dp", SEQ_AXES, None)
    in_specs = (rows, rows, rows, P("dp"), P(), P(SEQ_AXES, "dp"))
    return jax.shard_map(body, mesh=fine, in_specs=in_specs, out_specs=rows, check_vma=False)
```

```python
import jax
import jax.numpy as jnp
import numpy as np
from jax import lax
from jax.sharding import Mesh
from jax.sharding import PartitionSpec as P

HEADS = 16
HEAD = 128
BLOCK = 128

SEQ_AXES = ("z", "x", "c")


def exclusive_cumsum(stack):
    running = jnp.cumsum(stack, axis=0)
    return jnp.concatenate([jnp.zeros_like(stack[:1]), running[:-1]], axis=0), running[-1]


def swap_cores(x):
    return lax.ppermute(x, "c", [(0, 1), (1, 0)])


def prefix_of(own):
    xi, ci = lax.axis_index("x"), lax.axis_index("c")
    nz, nx, nc = (lax.axis_size(a) for a in SEQ_AXES)
    assert nc == 2
    partner = swap_cores(own)
    chip_total = own + partner
    within_chip = jnp.where(ci == 1, partner, jnp.zeros_like(partner))
    half = HEADS // nc
    quarter = half // nx
    mine = lax.dynamic_slice_in_dim(chip_total, ci * half, half, 0)
    by_chip = lax.all_to_all(mine.reshape(nx, quarter, HEAD, HEAD), "x", 0, 0)
    before_in_row, row_total = exclusive_cumsum(by_chip)
    pieces = row_total.reshape(nz, quarter * HEAD // nz, HEAD)
    by_row = lax.all_to_all(pieces, "z", 0, 0)
    before_rows, _ = exclusive_cumsum(by_row)
    before_rows = lax.all_to_all(before_rows, "z", 0, 0).reshape(quarter, HEAD, HEAD)
    back = lax.all_to_all(before_in_row + before_rows[None], "x", 0, 0)
    mine = back.reshape(half, HEAD, HEAD)
    theirs = swap_cores(mine)
    chip_prefix = jnp.where(
        ci == 0,
        jnp.concatenate([mine, theirs], axis=0),
        jnp.concatenate([theirs, mine], axis=0),
    )
    return chip_prefix + within_chip


def body(queries, keys, values, lengths, norm_gain, out_weight):
    nz, nx, nc = (lax.axis_size(a) for a in SEQ_AXES)
    query_doc = queries[0]
    tok = query_doc.shape[0]
    nblk = tok // BLOCK
    shape = (nblk, BLOCK, HEADS, HEAD)
    query_blocks = query_doc.reshape(shape)
    key_blocks = keys[0].reshape(shape)
    value_blocks = values[0].reshape(shape)
    high = lax.Precision.HIGHEST
    block_state = jnp.einsum(
        "nshd,nshe->nhde", key_blocks, value_blocks, preferred_element_type=jnp.float32
    )
    own_state = jnp.sum(block_state, axis=0)
    prefix = prefix_of(own_state)
    running = jnp.cumsum(block_state, axis=0)
    earlier = jnp.concatenate(
        [jnp.zeros((1, HEADS, HEAD, HEAD), jnp.float32), running[:-1]], axis=0
    )
    prior_state = prefix[None] + earlier
    causal = jnp.arange(BLOCK)[:, None] >= jnp.arange(BLOCK)[None, :]
    scores = jnp.einsum(
        "nthd,nshd->nhts", query_blocks, key_blocks, preferred_element_type=jnp.float32
    )
    scores = jnp.where(causal[None, None], scores, 0.0).astype(jnp.bfloat16)
    local = jnp.einsum("nhts,nshd->nthd", scores, value_blocks, preferred_element_type=jnp.float32)
    cross = jnp.einsum(
        "nthd,nhde->nthe", query_blocks.astype(jnp.float32), prior_state, precision=high
    )
    mixed = (local + cross).reshape(tok, HEADS, HEAD)
    meansq = jnp.mean(mixed * mixed, axis=-1, keepdims=True)
    normed = mixed * lax.rsqrt(meansq + 1e-06) * norm_gain.reshape(HEADS, HEAD)
    seq_index = lax.axis_index(SEQ_AXES)
    position = seq_index * tok + jnp.arange(tok)
    valid = position < lengths[0]
    normed = jnp.where(valid[:, None, None], normed, 0.0).astype(jnp.bfloat16)
    rows_per, cols_per = out_weight.shape
    ndp = lax.axis_size("dp")
    copies = jnp.broadcast_to(out_weight[None], (ndp, rows_per, cols_per))
    by_column = lax.all_to_all(copies, "dp", 0, 0)
    wide = jnp.transpose(by_column, (1, 0, 2)).reshape(rows_per, ndp * cols_per)
    weight = lax.all_gather(wide, SEQ_AXES, axis=0, tiled=True)
    normed = normed.reshape(tok, HEADS * HEAD)
    result = jnp.dot(normed, weight, preferred_element_type=jnp.float32)
    return result.astype(jnp.bfloat16)[None]


def solution(mesh, nx=4, ncore=2):
    ndp, nseq = mesh.devices.shape
    devices = np.asarray(mesh.devices).reshape(ndp, nseq // (nx * ncore), nx, ncore)
    fine = Mesh(devices, ("dp",) + SEQ_AXES)
    rows = P("dp", SEQ_AXES, None)
    in_specs = (rows, rows, rows, P("dp"), P(), P(SEQ_AXES, "dp"))
    return jax.shard_map(body, mesh=fine, in_specs=in_specs, out_specs=rows, check_vma=False)
```
